128 devices in a mesh: path: 16 (over x, y_lo, core), trade: 8 (over y_hi, z).
Axes of the slice: x: 4, y: 4 (y_hi: 2, y_lo: 2; y = y_hi * 2 + y_lo), z: 4, core: 2. Of those that a mesh axis runs over, the one named last changes fastest.
Arguments:
- factors: bfloat16 [65536, 256], P('path'), may hold values from -6 to 6
- exposures: bfloat16 [16384, 256], P('trade'), may hold values from -0.375 to 0.375
- strikes: float32 [16384], P('trade'), may hold values from -1 to 1
- notionals: float32 [16384], P('trade'), may hold values from -0.09375 to 0.09375
- w_first: float32 [256, 1024], replicated, may hold values from -0.375 to 0.375
- b_first: float32 [1024], replicated, may hold values from -3 to 3
- w_second: float32 [1024, 1024], replicated, may hold values from -0.1875 to 0.1875
- b_second: float32 [1024], replicated, may hold values from -3 to 3
- w_out: float32 [1024], replicated, may hold values from -0.1875 to 0.1875
- b_out: float32 [1], replicated, may hold values from -3 to 3
Outputs:
- grad_w_first: float32 [256, 1024], replicated
- grad_b_first: float32 [1024], replicated
- grad_w_second: float32 [1024, 1024], replicated
- grad_b_second: float32 [1024], replicated
- grad_w_out: float32 [1024], replicated
- grad_b_out: float32 [1], replicated
The draws below stay inside these ranges and needn't reach their ends.
All inputs are finite; a program needn't handle non-finite values.
Results may differ from the reference program's by a relative error of at most 0.0003.
Values sent between devices are 32-bit elements; how exact they have to be, the bound alone decides.
No kernel may reach another device: no remote copies, remote signals or barrier semaphores. Data moves between devices by JAX's collectives and lax.ppermute only.
A program may use at most 128 MiB of HBM per device.

```python
import jax
import jax.numpy as jnp
from jax import lax

FACTORS = 256
HIDDEN_SIZE = 1024
PATHS = 65536
TRADES = 16384


def block_levels(key, shape, cuts, low, largest):
    loudness = 1.0
    for axis_at, parts in cuts:
        heights = jax.random.uniform(jax.random.fold_in(jax.random.fold_in(key, 6), axis_at), (parts,), jnp.float32, low / len(cuts), largest / len(cuts))
        loudness = loudness * jnp.repeat(jnp.exp(heights), shape[axis_at] // parts).reshape((-1,) + (1,) * (len(shape) - 1 - axis_at))
    return loudness


def gaussian(stream_key, dims, scale, reach, shards=(), dtype=jnp.bfloat16):
    result = jax.random.normal(stream_key, dims, jnp.float32) * scale
    if len(shards) > 0:
        result = block_levels(stream_key, dims, shards, -0.22, 0.18) * result
    return jnp.clip(result, min=-reach, max=reach).astype(dtype)


def setup_inputs(seed: int = 0) -> dict:
    keys = jax.random.split(jax.random.key(seed), 11)
    factors = gaussian(keys[0], (PATHS, FACTORS), 1.0, 6.0, ((0, 16),))
    exposures = gaussian(keys[1], (TRADES, FACTORS), FACTORS ** -0.5, 0.375, ((0, 8),))
    strikes = jnp.clip(jax.random.uniform(keys[2], (TRADES,), jnp.float32, -1.0, 1.0) * block_levels(keys[2], (TRADES,), ((0, 8),), -0.4, 0.0), -1.0, 1.0)
    notionals = gaussian(keys[3], (TRADES,), (TRADES // 4) ** -0.5, 0.09375, ((0, 8),), jnp.float32)
    w_first = gaussian(keys[4], (FACTORS, HIDDEN_SIZE), FACTORS ** -0.5, 0.375, (), jnp.float32)
    b_first = gaussian(keys[5], (HIDDEN_SIZE,), 0.5, 3.0, (), jnp.float32)
    w_second = gaussian(keys[6], (HIDDEN_SIZE, HIDDEN_SIZE), HIDDEN_SIZE ** -0.5, 0.1875, (), jnp.float32)
    b_second = gaussian(keys[7], (HIDDEN_SIZE,), 0.5, 3.0, (), jnp.float32)
    w_out = gaussian(keys[8], (HIDDEN_SIZE,), HIDDEN_SIZE ** -0.5, 0.1875, (), jnp.float32)
    b_out = gaussian(keys[9], (1,), 1.0, 3.0, (), jnp.float32)
    return dict(factors=factors, exposures=exposures, strikes=strikes, notionals=notionals, w_first=w_first, b_first=b_first, w_second=w_second, b_second=b_second, w_out=w_out, b_out=b_out)


def twin_loss(params, inputs, value, differential, scale):
    w_first, b_first, w_second, b_second, w_out, b_out = params
    highest = lax.Precision.HIGHEST
    act_one = jnp.dot(inputs, w_first, precision=highest) + b_first
    hid_one = jax.nn.softplus(act_one)
    act_two = jnp.dot(hid_one, w_second, precision=highest) + b_second
    hid_two = jax.nn.softplus(act_two)
    predicted = jnp.dot(hid_two, w_out, precision=highest) + b_out[0]
    back_two = w_out * jax.nn.sigmoid(act_two)
    back_one = jnp.dot(back_two, w_second.T, precision=highest) * jax.nn.sigmoid(act_one)
    slope = jnp.dot(back_one, w_first.T, precision=highest)
    miss_value = predicted - value
    miss_slope = slope - differential
    return (jnp.sum(miss_value * miss_value) + jnp.sum(miss_slope * miss_slope)) * scale

def reference(factors, exposures, strikes, notionals, w_first, b_first, w_second, b_second, w_out, b_out):
    paths, width = factors.shape
    trades = exposures.shape[0]
    block_len = min(512, trades)
    count = trades // block_len
    expo_blocks = exposures.reshape(count, block_len, width)
    strike_blocks = strikes.reshape(count, block_len)
    notional_blocks = notionals.reshape(count, block_len)

    def add_block(carry, block):
        value, differential = carry
        expo, strike, notional = block
        moneyness = jnp.einsum('pf,tf->pt', factors, expo, preferred_element_type=jnp.float32) - strike
        value = value + jnp.dot(jax.nn.softplus(moneyness), notional, precision=lax.Precision.HIGHEST)
        weighting = (jax.nn.sigmoid(moneyness) * notional).astype(jnp.bfloat16)
        differential = differential + jnp.dot(weighting, expo, preferred_element_type=jnp.float32)
        return ((value, differential), None)
    start = (jnp.zeros((paths,), jnp.float32), jnp.zeros((paths, width), jnp.float32))
    (value, differential), _ = lax.scan(add_block, start, (expo_blocks, strike_blocks, notional_blocks))
    inputs = factors.astype(jnp.float32)
    scale = 1.0 / jnp.sqrt(jnp.float32(paths))
    params = (w_first, b_first, w_second, b_second, w_out, b_out)
    grads = jax.grad(twin_loss)(params, inputs, value, differential, scale)
    return (grads[0], grads[1], grads[2], grads[3], grads[4], grads[5])
```

```python
import jax
import jax.numpy as jnp
from jax import lax
from jax.sharding import PartitionSpec as P


def twin_loss(params, inputs, value, differential, scale):
    w_first, b_first, w_second, b_second, w_out, b_out = params
    highest = lax.Precision.HIGHEST
    act_one = jnp.dot(inputs, w_first, precision=highest) + b_first
    hid_one = jax.nn.softplus(act_one)
    act_two = jnp.dot(hid_one, w_second, precision=highest) + b_second
    hid_two = jax.nn.softplus(act_two)
    predicted = jnp.dot(hid_two, w_out, precision=highest) + b_out[0]
    back_two = w_out * jax.nn.sigmoid(act_two)
    back_one = jnp.dot(back_two, w_second.T, precision=highest) * jax.nn.sigmoid(act_one)
    slope = jnp.dot(back_one, w_first.T, precision=highest)
    miss_value = predicted - value
    miss_slope = slope - differential
    return (jnp.sum(miss_value * miss_value) + jnp.sum(miss_slope * miss_slope)) * scale


def body(
    factors, exposures, strikes, notionals, w_first, b_first, w_second, b_second, w_out, b_out
):
    paths, width = factors.shape
    trades = exposures.shape[0]
    block_len = min(512, trades)
    count = trades // block_len
    expo_blocks = exposures.reshape(count, block_len, width)
    strike_blocks = strikes.reshape(count, block_len)
    notional_blocks = notionals.reshape(count, block_len)

    def add_block(carry, block):
        value, differential = carry
        expo, strike, notional = block
        moneyness = (
            jnp.einsum("pf,tf->pt", factors, expo, preferred_element_type=jnp.float32) - strike
        )
        value = value + jnp.dot(
            jax.nn.softplus(moneyness), notional, precision=lax.Precision.HIGHEST
        )
        weighting = (jax.nn.sigmoid(moneyness) * notional).astype(jnp.bfloat16)
        differential = differential + jnp.dot(weighting, expo, preferred_element_type=jnp.float32)
        return ((value, differential), None)

    start = (jnp.zeros((paths,), jnp.float32), jnp.zeros((paths, width), jnp.float32))
    (value, differential), _ = lax.scan(
        add_block, start, (expo_blocks, strike_blocks, notional_blocks)
    )
    groups = lax.axis_size("trade")
    own_rows = paths // groups
    first_row = lax.axis_index("trade") * own_rows
    value_rows = -(-own_rows // width)
    value_pad = jnp.pad(value.reshape(groups, own_rows), ((0, 0), (0, value_rows * width - own_rows)))
    packed = jnp.concatenate(
        [differential.reshape(groups, own_rows, width), value_pad.reshape(groups, value_rows, width)],
        axis=1,
    )
    mine = lax.psum_scatter(packed, "trade", scatter_dimension=0, tiled=False)
    my_diff = mine[:own_rows]
    my_value = mine[own_rows:].reshape(-1)[:own_rows]
    my_inputs = lax.dynamic_slice_in_dim(factors, first_row, own_rows, 0).astype(jnp.float32)
    scale = 1.0 / jnp.sqrt(jnp.float32(paths * lax.axis_size("path")))
    params = (w_first, b_first, w_second, b_second, w_out, b_out)
    grads = jax.grad(twin_loss)(params, my_inputs, my_value, my_diff, scale)
    hidden = w_second.shape[0]
    small = jnp.stack([grads[1], grads[3], grads[4], jnp.pad(grads[5], (0, hidden - 1))])
    flat = jnp.concatenate([grads[0], grads[2], small], axis=0)
    flat = lax.psum(flat, ("path", "trade"))
    n0 = w_first.shape[0]
    g0 = flat[:n0]
    g2 = flat[n0 : n0 + hidden]
    tail = flat[n0 + hidden :]
    return (g0, tail[0], g2, tail[1], tail[2], tail[3, :1])


def solution(mesh):
    in_specs = (
        P("path", None),
        P("trade", None),
        P("trade"),
        P("trade"),
        P(),
        P(),
        P(),
        P(),
        P(),
        P(),
    )
    out_specs = (P(), P(), P(), P(), P(), P())
    return jax.shard_map(body, mesh=mesh, in_specs=in_specs, out_specs=out_specs, check_vma=False)
```

```python
import jax
import jax.numpy as jnp
from jax import lax
from jax.sharding import PartitionSpec as P


def twin_loss(params, inputs, value, differential, scale):
    w_first, b_first, w_second, b_second, w_out, b_out = params
    highest = lax.Precision.HIGH
    act_one = jnp.dot(inputs, w_first, precision=highest) + b_first
    hid_one = jax.nn.softplus(act_one)
    act_two = jnp.dot(hid_one, w_second, precision=highest) + b_second
    hid_two = jax.nn.softplus(act_two)
    predicted = jnp.dot(hid_two, w_out, precision=highest) + b_out[0]
    back_two = w_out * jax.nn.sigmoid(act_two)
    back_one = jnp.dot(back_two, w_second.T, precision=highest) * jax.nn.sigmoid(act_one)
    slope = jnp.dot(back_one, w_first.T, precision=highest)
    miss_value = predicted - value
    miss_slope = slope - differential
    return (jnp.sum(miss_value * miss_value) + jnp.sum(miss_slope * miss_slope)) * scale


def body(
    factors, exposures, strikes, notionals, w_first, b_first, w_second, b_second, w_out, b_out
):
    paths, width = factors.shape
    trades = exposures.shape[0]
    block_len = min(512, trades)
    count = trades // block_len
    expo_blocks = exposures.reshape(count, block_len, width)
    strike_blocks = strikes.reshape(count, block_len)
    notional_blocks = notionals.reshape(count, block_len)

    def add_block(carry, block):
        value, differential = carry
        expo, strike, notional = block
        moneyness = (
            jnp.einsum("pf,tf->pt", factors, expo, preferred_element_type=jnp.float32) - strike
        )
        value = value + jnp.dot(
            jax.nn.softplus(moneyness), notional, precision=lax.Precision.HIGHEST
        )
        weighting = (jax.nn.sigmoid(moneyness) * notional).astype(jnp.bfloat16)
        differential = differential + jnp.dot(weighting, expo, preferred_element_type=jnp.float32)
        return ((value, differential), None)

    start = (jnp.zeros((paths,), jnp.float32), jnp.zeros((paths, width), jnp.float32))
    (value, differential), _ = lax.scan(
        add_block, start, (expo_blocks, strike_blocks, notional_blocks)
    )
    groups = lax.axis_size("trade")
    own_rows = paths // groups
    first_row = lax.axis_index("trade") * own_rows
    value_rows = -(-own_rows // width)
    value_pad = jnp.pad(value.reshape(groups, own_rows), ((0, 0), (0, value_rows * width - own_rows)))
    packed = jnp.concatenate(
        [differential.reshape(groups, own_rows, width), value_pad.reshape(groups, value_rows, width)],
        axis=1,
    )
    mine = lax.psum_scatter(packed, "trade", scatter_dimension=0, tiled=False)
    my_diff = mine[:own_rows]
    my_value = mine[own_rows:].reshape(-1)[:own_rows]
    my_inputs = lax.dynamic_slice_in_dim(factors, first_row, own_rows, 0).astype(jnp.float32)
    scale = 1.0 / jnp.sqrt(jnp.float32(paths * lax.axis_size("path")))
    params = (w_first, b_first, w_second, b_second, w_out, b_out)
    grads = jax.grad(twin_loss)(params, my_inputs, my_value, my_diff, scale)
    hidden = w_second.shape[0]
    small = jnp.stack([grads[1], grads[3], grads[4], jnp.pad(grads[5], (0, hidden - 1))])
    head = jnp.concatenate([grads[0], small], axis=0)
    head, g2 = lax.psum((head, grads[2]), ("path", "trade"))
    n0 = w_first.shape[0]
    g0 = head[:n0]
    tail = head[n0:]
    return (g0, tail[0], g2, tail[1], tail[2], tail[3, :1])

def solution(mesh):
    in_specs = (
        P("path", None),
        P("trade", None),
        P("trade"),
        P("trade"),
        P(),
        P(),
        P(),
        P(),
        P(),
        P(),
    )
    out_specs = (P(), P(), P(), P(), P(), P())
    return jax.shard_map(body, mesh=mesh, in_specs=in_specs, out_specs=out_specs, check_vma=False)
```

```python
import jax
import jax.numpy as jnp
from jax import lax
from jax.sharding import PartitionSpec as P
from jax.experimental import pallas as pl
from jax.experimental.pallas import tpu as pltpu


def twin_loss(params, inputs, value, differential, scale):
    w_first, b_first, w_second, b_second, w_out, b_out = params
    highest = lax.Precision.HIGH
    act_one = jnp.dot(inputs, w_first, precision=highest) + b_first
    hid_one = jax.nn.softplus(act_one)
    act_two = jnp.dot(hid_one, w_second, precision=highest) + b_second
    hid_two = jax.nn.softplus(act_two)
    predicted = jnp.dot(hid_two, w_out, precision=highest) + b_out[0]
    back_two = w_out * jax.nn.sigmoid(act_two)
    back_one = jnp.dot(back_two, w_second.T, precision=highest) * jax.nn.sigmoid(act_one)
    slope = jnp.dot(back_one, w_first.T, precision=highest)
    miss_value = predicted - value
    miss_slope = slope - differential
    return (jnp.sum(miss_value * miss_value) + jnp.sum(miss_slope * miss_slope)) * scale


ROW_CHUNK = 16
LANE_CHUNK = 256


def price_kernel(f_ref, e_ref, s_ref, n_ref, d_ref, v_ref, m_scr, w_scr):
    m_scr[...] = lax.dot_general(
        f_ref[...], e_ref[...], (((1,), (1,)), ((), ())), preferred_element_type=jnp.float32
    )
    tile, trades = m_scr.shape

    def rows(i, carry):
        r = pl.multiple_of(i * ROW_CHUNK, ROW_CHUNK)
        acc = jnp.zeros((ROW_CHUNK, 128), jnp.float32)
        for c in range(trades // LANE_CHUNK):
            cs = slice(c * LANE_CHUNK, (c + 1) * LANE_CHUNK)
            m = m_scr[pl.ds(r, ROW_CHUNK), cs] - s_ref[:, cs]
            notional = n_ref[:, cs]
            e = jnp.exp(-jnp.abs(m))
            soft = jnp.maximum(m, 0.0) + jnp.log1p(e)
            rcp = 1.0 / (1.0 + e)
            sig = jnp.where(m >= 0.0, rcp, e * rcp)
            w_scr[pl.ds(r, ROW_CHUNK), cs] = (sig * notional).astype(jnp.bfloat16)
            t = soft * notional
            for g in range(LANE_CHUNK // 128):
                acc = acc + t[:, g * 128 : (g + 1) * 128]
        v_ref[pl.ds(r, ROW_CHUNK), :] = acc
        return carry

    lax.fori_loop(0, tile // ROW_CHUNK, rows, 0)
    d_ref[...] = jnp.dot(w_scr[...], e_ref[...], preferred_element_type=jnp.float32)


def price(factors, exposures, strikes, notionals, tile=256):
    paths, width = factors.shape
    trades = exposures.shape[0]
    return pl.pallas_call(
        price_kernel,
        grid=(paths // tile,),
        in_specs=[
            pl.BlockSpec((tile, width), lambda i: (i, 0)),
            pl.BlockSpec((trades, width), lambda i: (0, 0)),
            pl.BlockSpec((1, trades), lambda i: (0, 0)),
            pl.BlockSpec((1, trades), lambda i: (0, 0)),
        ],
        out_specs=[
            pl.BlockSpec((tile, width), lambda i: (i, 0)),
            pl.BlockSpec((tile, 128), lambda i: (i, 0)),
        ],
        out_shape=[
            jax.ShapeDtypeStruct((paths, width), jnp.float32),
            jax.ShapeDtypeStruct((paths, 128), jnp.float32),
        ],
        scratch_shapes=[
            pltpu.VMEM((tile, trades), jnp.float32),
            pltpu.VMEM((tile, trades), jnp.bfloat16),
        ],
    )(factors, exposures, strikes.reshape(1, trades), notionals.reshape(1, trades))


def body(
    factors, exposures, strikes, notionals, w_first, b_first, w_second, b_second, w_out, b_out
):
    paths, width = factors.shape
    with jax.named_scope("price_trades"):
        differential, value_parts = price(factors, exposures, strikes, notionals)
    value = jnp.sum(value_parts, axis=1)
    groups = lax.axis_size("trade")
    own_rows = paths // groups
    first_row = lax.axis_index("trade") * own_rows
    value_rows = -(-own_rows // width)
    value_pad = jnp.pad(value.reshape(groups, own_rows), ((0, 0), (0, value_rows * width - own_rows)))
    packed = jnp.concatenate(
        [differential.reshape(groups, own_rows, width), value_pad.reshape(groups, value_rows, width)],
        axis=1,
    )
    mine = lax.psum_scatter(packed, "trade", scatter_dimension=0, tiled=False)
    my_diff = mine[:own_rows]
    my_value = mine[own_rows:].reshape(-1)[:own_rows]
    my_inputs = lax.dynamic_slice_in_dim(factors, first_row, own_rows, 0).astype(jnp.float32)
    scale = 1.0 / jnp.sqrt(jnp.float32(paths * lax.axis_size("path")))
    params = (w_first, b_first, w_second, b_second, w_out, b_out)
    grads = jax.grad(twin_loss)(params, my_inputs, my_value, my_diff, scale)
    hidden = w_second.shape[0]
    small = jnp.stack([grads[1], grads[3], grads[4], jnp.pad(grads[5], (0, hidden - 1))])
    head = jnp.concatenate([grads[0], small], axis=0)
    head, g2 = lax.psum((head, grads[2]), ("path", "trade"))
    n0 = w_first.shape[0]
    g0 = head[:n0]
    tail = head[n0:]
    return (g0, tail[0], g2, tail[1], tail[2], tail[3, :1])

def solution(mesh):
    in_specs = (
        P("path", None),
        P("trade", None),
        P("trade"),
        P("trade"),
        P(),
        P(),
        P(),
        P(),
        P(),
        P(),
    )
    out_specs = (P(), P(), P(), P(), P(), P())
    return jax.shard_map(body, mesh=mesh, in_specs=in_specs, out_specs=out_specs, check_vma=False)
```

```python
import jax
import jax.numpy as jnp
from jax import lax
from jax.sharding import PartitionSpec as P
from jax.experimental import pallas as pl
from jax.experimental.pallas import tpu as pltpu


def twin_loss(params, inputs, value, differential, scale):
    w_first, b_first, w_second, b_second, w_out, b_out = params
    highest = lax.Precision.HIGH
    act_one = jnp.dot(inputs, w_first, precision=highest) + b_first
    hid_one = jax.nn.softplus(act_one)
    act_two = jnp.dot(hid_one, w_second, precision=highest) + b_second
    hid_two = jax.nn.softplus(act_two)
    predicted = jnp.dot(hid_two, w_out, precision=highest) + b_out[0]
    back_two = w_out * jax.nn.sigmoid(act_two)
    back_one = jnp.dot(back_two, w_second.T, precision=highest) * jax.nn.sigmoid(act_one)
    slope = jnp.dot(back_one, w_first.T, precision=highest)
    miss_value = predicted - value
    miss_slope = slope - differential
    return (jnp.sum(miss_value * miss_value) + jnp.sum(miss_slope * miss_slope)) * scale


ROW_CHUNK = 16
LANE_CHUNK = 256


def price_kernel(f_ref, e_ref, s_ref, n_ref, d_ref, v_ref, m_scr, w_scr):
    m_scr[...] = lax.dot_general(
        f_ref[...], e_ref[...], (((1,), (1,)), ((), ())), preferred_element_type=jnp.float32
    )
    tile, trades = m_scr.shape

    def rows(i, carry):
        r = pl.multiple_of(i * ROW_CHUNK, ROW_CHUNK)
        acc = jnp.zeros((ROW_CHUNK, 128), jnp.float32)
        for c in range(trades // LANE_CHUNK):
            cs = slice(c * LANE_CHUNK, (c + 1) * LANE_CHUNK)
            m = m_scr[pl.ds(r, ROW_CHUNK), cs] - s_ref[:, cs]
            notional = n_ref[:, cs]
            e = jnp.exp(-jnp.abs(m))
            soft = jnp.maximum(m, 0.0) + jnp.log1p(e)
            rcp = 1.0 / (1.0 + e)
            sig = jnp.where(m >= 0.0, rcp, e * rcp)
            w_scr[pl.ds(r, ROW_CHUNK), cs] = (sig * notional).astype(jnp.bfloat16)
            t = soft * notional
            for g in range(LANE_CHUNK // 128):
                acc = acc + t[:, g * 128 : (g + 1) * 128]
        v_ref[pl.ds(r, ROW_CHUNK), :] = acc
        return carry

    lax.fori_loop(0, tile // ROW_CHUNK, rows, 0)
    d_ref[...] = jnp.dot(w_scr[...], e_ref[...], preferred_element_type=jnp.float32)


def price(factors, exposures, strikes, notionals, half, halves, tile=256):
    paths, width = factors.shape
    paths = paths // halves
    trades = exposures.shape[0]
    return pl.pallas_call(
        price_kernel,
        grid=(paths // tile,),
        in_specs=[
            pl.BlockSpec((tile, width), lambda i: (i * halves + half, 0)),
            pl.BlockSpec((trades, width), lambda i: (0, 0)),
            pl.BlockSpec((1, trades), lambda i: (0, 0)),
            pl.BlockSpec((1, trades), lambda i: (0, 0)),
        ],
        out_specs=[
            pl.BlockSpec((tile, width), lambda i: (i, 0)),
            pl.BlockSpec((tile, 128), lambda i: (i, 0)),
        ],
        out_shape=[
            jax.ShapeDtypeStruct((paths, width), jnp.float32),
            jax.ShapeDtypeStruct((paths, 128), jnp.float32),
        ],
        scratch_shapes=[
            pltpu.VMEM((tile, trades), jnp.float32),
            pltpu.VMEM((tile, trades), jnp.bfloat16),
        ],
    )(factors, exposures, strikes.reshape(1, trades), notionals.reshape(1, trades))


def body(
    factors, exposures, strikes, notionals, w_first, b_first, w_second, b_second, w_out, b_out
):
    paths, width = factors.shape
    groups = lax.axis_size("trade")
    own_rows = paths // groups
    first_row = lax.axis_index("trade") * own_rows
    halves = 2
    part_rows = own_rows // halves
    diff_parts, value_parts = [], []
    for half in range(halves):
        with jax.named_scope("price_trades"):
            diff_h, vpart_h = price(factors, exposures, strikes, notionals, half, halves)
        value_h = jnp.sum(vpart_h, axis=1).reshape(groups, 1, part_rows)
        packed = jnp.concatenate([diff_h.reshape(groups, part_rows, width), value_h], axis=1)
        mine = lax.psum_scatter(packed, "trade", scatter_dimension=0, tiled=False)
        diff_parts.append(mine[:part_rows])
        value_parts.append(mine[part_rows])
    my_diff = jnp.concatenate(diff_parts, axis=0)
    my_value = jnp.concatenate(value_parts, axis=0)
    my_inputs = lax.dynamic_slice_in_dim(factors, first_row, own_rows, 0).astype(jnp.float32)
    scale = 1.0 / jnp.sqrt(jnp.float32(paths * lax.axis_size("path")))
    params = (w_first, b_first, w_second, b_second, w_out, b_out)
    grads = jax.grad(twin_loss)(params, my_inputs, my_value, my_diff, scale)
    hidden = w_second.shape[0]
    small = jnp.stack([grads[1], grads[3], grads[4], jnp.pad(grads[5], (0, hidden - 1))])
    head = jnp.concatenate([grads[0], small], axis=0)
    head, g2 = lax.psum((head, grads[2]), ("path", "trade"))
    n0 = w_first.shape[0]
    g0 = head[:n0]
    tail = head[n0:]
    return (g0, tail[0], g2, tail[1], tail[2], tail[3, :1])

def solution(mesh):
    in_specs = (
        P("path", None),
        P("trade", None),
        P("trade"),
        P("trade"),
        P(),
        P(),
        P(),
        P(),
        P(),
        P(),
    )
    out_specs = (P(), P(), P(), P(), P(), P())
    return jax.shard_map(body, mesh=mesh, in_specs=in_specs, out_specs=out_specs, check_vma=False)
```

```python
import jax
import jax.numpy as jnp
from jax import lax
from jax.sharding import PartitionSpec as P
from jax.experimental import pallas as pl
from jax.experimental.pallas import tpu as pltpu


def twin_loss(params, inputs, value, differential, scale):
    w_first, b_first, w_second, b_second, w_out, b_out = params
    highest = lax.Precision.HIGH
    act_one = jnp.dot(inputs, w_first, precision=highest) + b_first
    hid_one = jax.nn.softplus(act_one)
    act_two = jnp.dot(hid_one, w_second, precision=highest) + b_second
    hid_two = jax.nn.softplus(act_two)
    predicted = jnp.dot(hid_two, w_out, precision=highest) + b_out[0]
    back_two = w_out * jax.nn.sigmoid(act_two)
    back_one = jnp.dot(back_two, w_second.T, precision=highest) * jax.nn.sigmoid(act_one)
    slope = jnp.dot(back_one, w_first.T, precision=highest)
    miss_value = predicted - value
    miss_slope = slope - differential
    return (jnp.sum(miss_value * miss_value) + jnp.sum(miss_slope * miss_slope)) * scale


ROW_CHUNK = 16
LANE_CHUNK = 256


def price_kernel(f_ref, e_ref, s_ref, n_ref, d_ref, v_ref, m_scr, w_scr):
    m_scr[...] = lax.dot_general(
        f_ref[...], e_ref[...], (((1,), (1,)), ((), ())), preferred_element_type=jnp.float32
    )
    tile, trades = m_scr.shape

    def rows(i, carry):
        r = pl.multiple_of(i * ROW_CHUNK, ROW_CHUNK)
        acc = jnp.zeros((ROW_CHUNK, 128), jnp.float32)
        for c in range(trades // LANE_CHUNK):
            cs = slice(c * LANE_CHUNK, (c + 1) * LANE_CHUNK)
            m = m_scr[pl.ds(r, ROW_CHUNK), cs] - s_ref[:, cs]
            notional = n_ref[:, cs]
            e = jnp.exp(-jnp.abs(m))
            soft = jnp.maximum(m, 0.0) + jnp.log1p(e)
            rcp = 1.0 / (1.0 + e)
            sig = jnp.where(m >= 0.0, rcp, e * rcp)
            w_scr[pl.ds(r, ROW_CHUNK), cs] = (sig * notional).astype(jnp.bfloat16)
            t = soft * notional
            for g in range(LANE_CHUNK // 128):
                acc = acc + t[:, g * 128 : (g + 1) * 128]
        v_ref[pl.ds(r, ROW_CHUNK), :] = acc
        return carry

    lax.fori_loop(0, tile // ROW_CHUNK, rows, 0)
    d_ref[...] = jnp.dot(w_scr[...], e_ref[...], preferred_element_type=jnp.float32)


def price(factors, exposures, strikes, notionals, tile=256):
    paths, width = factors.shape
    trades = exposures.shape[0]
    return pl.pallas_call(
        price_kernel,
        grid=(paths // tile,),
        in_specs=[
            pl.BlockSpec((tile, width), lambda i: (i, 0)),
            pl.BlockSpec((trades, width), lambda i: (0, 0)),
            pl.BlockSpec((1, trades), lambda i: (0, 0)),
            pl.BlockSpec((1, trades), lambda i: (0, 0)),
        ],
        out_specs=[
            pl.BlockSpec((tile, width), lambda i: (i, 0)),
            pl.BlockSpec((tile, 128), lambda i: (i, 0)),
        ],
        out_shape=[
            jax.ShapeDtypeStruct((paths, width), jnp.float32),
            jax.ShapeDtypeStruct((paths, 128), jnp.float32),
        ],
        scratch_shapes=[
            pltpu.VMEM((tile, trades), jnp.float32),
            pltpu.VMEM((tile, trades), jnp.bfloat16),
        ],
    )(factors, exposures, strikes.reshape(1, trades), notionals.reshape(1, trades))


def body(
    factors, exposures, strikes, notionals, w_first, b_first, w_second, b_second, w_out, b_out
):
    paths, width = factors.shape
    with jax.named_scope("price_trades"):
        differential, value_parts = price(factors, exposures, strikes, notionals)
    value = jnp.sum(value_parts, axis=1)
    groups = lax.axis_size("trade")
    own_rows = paths // groups
    first_row = lax.axis_index("trade") * own_rows
    value_rows = -(-own_rows // width)
    value_pad = jnp.pad(value.reshape(groups, own_rows), ((0, 0), (0, value_rows * width - own_rows)))
    packed = jnp.concatenate(
        [differential.reshape(groups, own_rows, width), value_pad.reshape(groups, value_rows, width)],
        axis=1,
    )
    me = lax.axis_index("trade")
    z_len = groups // 2
    mine = lax.dynamic_index_in_dim(packed, me, 0, keepdims=False)
    for dy in range(2):
        for dz in range(z_len):
            if dy == 0 and dz == 0:
                continue

            def dest(t, dy=dy, dz=dz):
                return ((t // z_len + dy) % 2) * z_len + (t % z_len + dz) % z_len

            block = lax.dynamic_index_in_dim(packed, dest(me), 0, keepdims=False)
            mine = mine + lax.ppermute(block, "trade", [(t, dest(t)) for t in range(groups)])
    my_diff = mine[:own_rows]
    my_value = mine[own_rows:].reshape(-1)[:own_rows]
    my_inputs = lax.dynamic_slice_in_dim(factors, first_row, own_rows, 0).astype(jnp.float32)
    scale = 1.0 / jnp.sqrt(jnp.float32(paths * lax.axis_size("path")))
    params = (w_first, b_first, w_second, b_second, w_out, b_out)
    grads = jax.grad(twin_loss)(params, my_inputs, my_value, my_diff, scale)
    hidden = w_second.shape[0]
    small = jnp.stack([grads[1], grads[3], grads[4], jnp.pad(grads[5], (0, hidden - 1))])
    head = jnp.concatenate([grads[0], small], axis=0)
    head, g2 = lax.psum((head, grads[2]), ("path", "trade"))
    n0 = w_first.shape[0]
    g0 = head[:n0]
    tail = head[n0:]
    return (g0, tail[0], g2, tail[1], tail[2], tail[3, :1])

def solution(mesh):
    in_specs = (
        P("path", None),
        P("trade", None),
        P("trade"),
        P("trade"),
        P(),
        P(),
        P(),
        P(),
        P(),
        P(),
    )
    out_specs = (P(), P(), P(), P(), P(), P())
    return jax.shard_map(body, mesh=mesh, in_specs=in_specs, out_specs=out_specs, check_vma=False)
```

```python
import jax
import jax.numpy as jnp
from jax import lax
from jax.sharding import PartitionSpec as P
from jax.experimental import pallas as pl
from jax.experimental.pallas import tpu as pltpu


def twin_loss(params, inputs, value, differential, scale):
    w_first, b_first, w_second, b_second, w_out, b_out = params
    highest = lax.Precision.HIGH
    act_one = jnp.dot(inputs, w_first, precision=highest) + b_first
    hid_one = jax.nn.softplus(act_one)
    act_two = jnp.dot(hid_one, w_second, precision=highest) + b_second
    hid_two = jax.nn.softplus(act_two)
    predicted = jnp.dot(hid_two, w_out, precision=highest) + b_out[0]
    back_two = w_out * jax.nn.sigmoid(act_two)
    back_one = jnp.dot(back_two, w_second.T, precision=highest) * jax.nn.sigmoid(act_one)
    slope = jnp.dot(back_one, w_first.T, precision=highest)
    miss_value = predicted - value
    miss_slope = slope - differential
    return (jnp.sum(miss_value * miss_value) + jnp.sum(miss_slope * miss_slope)) * scale


ROW_CHUNK = 16
LANE_CHUNK = 256


def price_kernel(f_ref, e_ref, s_ref, n_ref, d_ref, v_ref, m_scr, w_scr):
    m_scr[...] = lax.dot_general(
        f_ref[...], e_ref[...], (((1,), (1,)), ((), ())), preferred_element_type=jnp.float32
    )
    tile, trades = m_scr.shape

    def rows(i, carry):
        r = pl.multiple_of(i * ROW_CHUNK, ROW_CHUNK)
        acc = jnp.zeros((ROW_CHUNK, 128), jnp.float32)
        for c in range(trades // LANE_CHUNK):
            cs = slice(c * LANE_CHUNK, (c + 1) * LANE_CHUNK)
            m = m_scr[pl.ds(r, ROW_CHUNK), cs] - s_ref[:, cs]
            notional = n_ref[:, cs]
            e = jnp.exp(-jnp.abs(m))
            soft = jnp.maximum(m, 0.0) + jnp.log1p(e)
            sig = jnp.exp(m - soft)
            w_scr[pl.ds(r, ROW_CHUNK), cs] = (sig * notional).astype(jnp.bfloat16)
            t = soft * notional
            for g in range(LANE_CHUNK // 128):
                acc = acc + t[:, g * 128 : (g + 1) * 128]
        v_ref[pl.ds(r, ROW_CHUNK), :] = acc
        return carry

    lax.fori_loop(0, tile // ROW_CHUNK, rows, 0)
    d_ref[...] = jnp.dot(w_scr[...], e_ref[...], preferred_element_type=jnp.float32)


def price(factors, exposures, strikes, notionals, tile=512):
    paths, width = factors.shape
    trades = exposures.shape[0]
    return pl.pallas_call(
        price_kernel,
        grid=(paths // tile,),
        in_specs=[
            pl.BlockSpec((tile, width), lambda i: (i, 0)),
            pl.BlockSpec((trades, width), lambda i: (0, 0)),
            pl.BlockSpec((1, trades), lambda i: (0, 0)),
            pl.BlockSpec((1, trades), lambda i: (0, 0)),
        ],
        out_specs=[
            pl.BlockSpec((tile, width), lambda i: (i, 0)),
            pl.BlockSpec((tile, 128), lambda i: (i, 0)),
        ],
        out_shape=[
            jax.ShapeDtypeStruct((paths, width), jnp.float32),
            jax.ShapeDtypeStruct((paths, 128), jnp.float32),
        ],
        scratch_shapes=[
            pltpu.VMEM((tile, trades), jnp.float32),
            pltpu.VMEM((tile, trades), jnp.bfloat16),
        ],
    )(factors, exposures, strikes.reshape(1, trades), notionals.reshape(1, trades))


def body(
    factors, exposures, strikes, notionals, w_first, b_first, w_second, b_second, w_out, b_out
):
    paths, width = factors.shape
    with jax.named_scope("price_trades"):
        differential, value_parts = price(factors, exposures, strikes, notionals)
    value = jnp.sum(value_parts, axis=1)
    groups = lax.axis_size("trade")
    own_rows = paths // groups
    first_row = lax.axis_index("trade") * own_rows
    value_rows = -(-own_rows // width)
    value_pad = jnp.pad(value.reshape(groups, own_rows), ((0, 0), (0, value_rows * width - own_rows)))
    packed = jnp.concatenate(
        [differential.reshape(groups, own_rows, width), value_pad.reshape(groups, value_rows, width)],
        axis=1,
    )
    me = lax.axis_index("trade")
    z_len = groups // 2
    mine = lax.dynamic_index_in_dim(packed, me, 0, keepdims=False)
    for dy in range(2):
        for dz in range(z_len):
            if dy == 0 and dz == 0:
                continue

            def dest(t, dy=dy, dz=dz):
                return ((t // z_len + dy) % 2) * z_len + (t % z_len + dz) % z_len

            block = lax.dynamic_index_in_dim(packed, dest(me), 0, keepdims=False)
            mine = mine + lax.ppermute(block, "trade", [(t, dest(t)) for t in range(groups)])
    my_diff = mine[:own_rows]
    my_value = mine[own_rows:].reshape(-1)[:own_rows]
    my_inputs = lax.dynamic_slice_in_dim(factors, first_row, own_rows, 0).astype(jnp.float32)
    scale = 1.0 / jnp.sqrt(jnp.float32(paths * lax.axis_size("path")))
    params = (w_first, b_first, w_second, b_second, w_out, b_out)
    grads = jax.grad(twin_loss)(params, my_inputs, my_value, my_diff, scale)
    hidden = w_second.shape[0]
    small = jnp.stack([grads[1], grads[3], grads[4], jnp.pad(grads[5], (0, hidden - 1))])
    head = jnp.concatenate([grads[0], small], axis=0)
    head, g2 = lax.psum((head, grads[2]), ("path", "trade"))
    n0 = w_first.shape[0]
    g0 = head[:n0]
    tail = head[n0:]
    return (g0, tail[0], g2, tail[1], tail[2], tail[3, :1])

def solution(mesh):
    in_specs = (
        P("path", None),
        P("trade", None),
        P("trade"),
        P("trade"),
        P(),
        P(),
        P(),
        P(),
        P(),
        P(),
    )
    out_specs = (P(), P(), P(), P(), P(), P())
    return jax.shard_map(body, mesh=mesh, in_specs=in_specs, out_specs=out_specs, check_vma=False)
```

```python
import jax
import jax.numpy as jnp
from jax import lax
from jax.sharding import PartitionSpec as P
from jax.experimental import pallas as pl
from jax.experimental.pallas import tpu as pltpu


def twin_loss(params, inputs, value, differential, scale):
    w_first, b_first, w_second, b_second, w_out, b_out = params
    highest = lax.Precision.HIGH
    act_one = jnp.dot(inputs, w_first, precision=highest) + b_first
    hid_one = jax.nn.softplus(act_one)
    act_two = jnp.dot(hid_one, w_second, precision=highest) + b_second
    hid_two = jax.nn.softplus(act_two)
    predicted = jnp.dot(hid_two, w_out, precision=highest) + b_out[0]
    back_two = w_out * jax.nn.sigmoid(act_two)
    back_one = jnp.dot(back_two, w_second.T, precision=highest) * jax.nn.sigmoid(act_one)
    slope = jnp.dot(back_one, w_first.T, precision=highest)
    miss_value = predicted - value
    miss_slope = slope - differential
    return (jnp.sum(miss_value * miss_value) + jnp.sum(miss_slope * miss_slope)) * scale


ROW_CHUNK = 16
LANE_CHUNK = 256


def price_kernel(f_ref, e_ref, s_ref, n_ref, d_ref, v_ref, m_scr, w_scr):
    m_scr[...] = lax.dot_general(
        f_ref[...], e_ref[...], (((1,), (1,)), ((), ())), preferred_element_type=jnp.float32
    )
    tile, trades = m_scr.shape

    def rows(i, carry):
        r = pl.multiple_of(i * ROW_CHUNK, ROW_CHUNK)
        acc = jnp.zeros((ROW_CHUNK, 128), jnp.float32)
        for c in range(trades // LANE_CHUNK):
            cs = slice(c * LANE_CHUNK, (c + 1) * LANE_CHUNK)
            m = m_scr[pl.ds(r, ROW_CHUNK), cs] - s_ref[:, cs]
            notional = n_ref[:, cs]
            e = jnp.exp(-jnp.abs(m))
            soft = jnp.maximum(m, 0.0) + jnp.log1p(e)
            sig = jnp.exp(m - soft)
            w_scr[pl.ds(r, ROW_CHUNK), cs] = (sig * notional).astype(jnp.bfloat16)
            t = soft * notional
            for g in range(LANE_CHUNK // 128):
                acc = acc + t[:, g * 128 : (g + 1) * 128]
        v_ref[pl.ds(r, ROW_CHUNK), :] = acc
        return carry

    lax.fori_loop(0, tile // ROW_CHUNK, rows, 0)
    d_ref[...] = jnp.dot(w_scr[...], e_ref[...], preferred_element_type=jnp.float32)


def price(factors, exposures, strikes, notionals, half, halves, tile):
    paths, width = factors.shape
    paths = paths // halves
    trades = exposures.shape[0]
    return pl.pallas_call(
        price_kernel,
        grid=(paths // tile,),
        in_specs=[
            pl.BlockSpec((tile, width), lambda i: (i * halves + half, 0)),
            pl.BlockSpec((trades, width), lambda i: (0, 0)),
            pl.BlockSpec((1, trades), lambda i: (0, 0)),
            pl.BlockSpec((1, trades), lambda i: (0, 0)),
        ],
        out_specs=[
            pl.BlockSpec((tile, width), lambda i: (i, 0)),
            pl.BlockSpec((tile, 128), lambda i: (i, 0)),
        ],
        out_shape=[
            jax.ShapeDtypeStruct((paths, width), jnp.float32),
            jax.ShapeDtypeStruct((paths, 128), jnp.float32),
        ],
        scratch_shapes=[
            pltpu.VMEM((tile, trades), jnp.float32),
            pltpu.VMEM((tile, trades), jnp.bfloat16),
        ],
    )(factors, exposures, strikes.reshape(1, trades), notionals.reshape(1, trades))


def body(
    factors, exposures, strikes, notionals, w_first, b_first, w_second, b_second, w_out, b_out
):
    paths, width = factors.shape
    groups = lax.axis_size("trade")
    own_rows = paths // groups
    first_row = lax.axis_index("trade") * own_rows
    halves = 2
    part_rows = own_rows // halves
    me = lax.axis_index("trade")
    z_len = groups // 2
    diff_parts, value_parts = [], []
    for half in range(halves):
        with jax.named_scope("price_trades"):
            diff_h, vpart_h = price(factors, exposures, strikes, notionals, half, halves, part_rows)
        value_h = jnp.sum(vpart_h, axis=1).reshape(groups, 1, part_rows)
        packed = jnp.concatenate([diff_h.reshape(groups, part_rows, width), value_h], axis=1)
        mine = lax.dynamic_index_in_dim(packed, me, 0, keepdims=False)
        for dy in range(2):
            for dz in range(z_len):
                if dy == 0 and dz == 0:
                    continue

                def dest(t, dy=dy, dz=dz):
                    return ((t // z_len + dy) % 2) * z_len + (t % z_len + dz) % z_len

                block = lax.dynamic_index_in_dim(packed, dest(me), 0, keepdims=False)
                mine = mine + lax.ppermute(block, "trade", [(t, dest(t)) for t in range(groups)])
        diff_parts.append(mine[:part_rows])
        value_parts.append(mine[part_rows])
    my_diff = jnp.concatenate(diff_parts, axis=0)
    my_value = jnp.concatenate(value_parts, axis=0)
    my_inputs = lax.dynamic_slice_in_dim(factors, first_row, own_rows, 0).astype(jnp.float32)
    scale = 1.0 / jnp.sqrt(jnp.float32(paths * lax.axis_size("path")))
    params = (w_first, b_first, w_second, b_second, w_out, b_out)
    grads = jax.grad(twin_loss)(params, my_inputs, my_value, my_diff, scale)
    hidden = w_second.shape[0]
    small = jnp.stack([grads[1], grads[3], grads[4], jnp.pad(grads[5], (0, hidden - 1))])
    head = jnp.concatenate([grads[0], small], axis=0)
    head, g2 = lax.psum((head, grads[2]), ("path", "trade"))
    n0 = w_first.shape[0]
    g0 = head[:n0]
    tail = head[n0:]
    return (g0, tail[0], g2, tail[1], tail[2], tail[3, :1])

def solution(mesh):
    in_specs = (
        P("path", None),
        P("trade", None),
        P("trade"),
        P("trade"),
        P(),
        P(),
        P(),
        P(),
        P(),
        P(),
    )
    out_specs = (P(), P(), P(), P(), P(), P())
    return jax.shard_map(body, mesh=mesh, in_specs=in_specs, out_specs=out_specs, check_vma=False)
```

```python
import jax
import jax.numpy as jnp
from jax import lax
from jax.sharding import PartitionSpec as P
from jax.experimental import pallas as pl
from jax.experimental.pallas import tpu as pltpu


def twin_loss(params, inputs, value, differential, scale):
    w_first, b_first, w_second, b_second, w_out, b_out = params
    highest = lax.Precision.HIGH
    act_one = jnp.dot(inputs, w_first, precision=highest) + b_first
    hid_one = jax.nn.softplus(act_one)
    act_two = jnp.dot(hid_one, w_second, precision=highest) + b_second
    hid_two = jax.nn.softplus(act_two)
    predicted = jnp.dot(hid_two, w_out, precision=highest) + b_out[0]
    back_two = w_out * jax.nn.sigmoid(act_two)
    back_one = jnp.dot(back_two, w_second.T, precision=highest) * jax.nn.sigmoid(act_one)
    slope = jnp.dot(back_one, w_first.T, precision=highest)
    miss_value = predicted - value
    miss_slope = slope - differential
    return (jnp.sum(miss_value * miss_value) + jnp.sum(miss_slope * miss_slope)) * scale


ROW_CHUNK = 16
LANE_CHUNK = 256


def price_kernel(f_ref, e_ref, s_ref, n_ref, d_ref, m_scr, w_scr, v_scr):
    m_scr[...] = lax.dot_general(
        f_ref[...], e_ref[...], (((1,), (1,)), ((), ())), preferred_element_type=jnp.float32
    )
    tile, trades = m_scr.shape

    def rows(i, carry):
        r = pl.multiple_of(i * ROW_CHUNK, ROW_CHUNK)
        acc = jnp.zeros((ROW_CHUNK, 128), jnp.float32)
        for c in range(trades // LANE_CHUNK):
            cs = slice(c * LANE_CHUNK, (c + 1) * LANE_CHUNK)
            m = m_scr[pl.ds(r, ROW_CHUNK), cs] - s_ref[:, cs]
            notional = n_ref[:, cs]
            e = jnp.exp(-jnp.abs(m))
            soft = jnp.maximum(m, 0.0) + jnp.log1p(e)
            sig = jnp.exp(m - soft)
            w_scr[pl.ds(r, ROW_CHUNK), cs] = (sig * notional).astype(jnp.bfloat16)
            t = soft * notional
            for g in range(LANE_CHUNK // 128):
                acc = acc + t[:, g * 128 : (g + 1) * 128]
        v_scr[pl.ds(r, ROW_CHUNK), :] = acc
        return carry

    lax.fori_loop(0, tile // ROW_CHUNK, rows, 0)
    width = e_ref.shape[1]
    d_ref[0, :tile, :] = jnp.dot(w_scr[...], e_ref[...], preferred_element_type=jnp.float32)
    value = jnp.sum(jnp.transpose(v_scr[...]), axis=0, keepdims=True)
    d_ref[0, tile:, :] = jnp.zeros((d_ref.shape[1] - tile, width), jnp.float32)
    for k in range(tile // width):
        d_ref[0, tile + k : tile + k + 1, :] = value[:, k * width : (k + 1) * width]


def price(factors, exposures, strikes, notionals, tile):
    paths, width = factors.shape
    trades = exposures.shape[0]
    extra = -(-(tile // width) // 8) * 8
    return pl.pallas_call(
        price_kernel,
        grid=(paths // tile,),
        in_specs=[
            pl.BlockSpec((tile, width), lambda i: (i, 0)),
            pl.BlockSpec((trades, width), lambda i: (0, 0)),
            pl.BlockSpec((1, trades), lambda i: (0, 0)),
            pl.BlockSpec((1, trades), lambda i: (0, 0)),
        ],
        out_specs=pl.BlockSpec((1, tile + extra, width), lambda i: (i, 0, 0)),
        out_shape=jax.ShapeDtypeStruct((paths // tile, tile + extra, width), jnp.float32),
        scratch_shapes=[
            pltpu.VMEM((tile, trades), jnp.float32),
            pltpu.VMEM((tile, trades), jnp.bfloat16),
            pltpu.VMEM((tile, 128), jnp.float32),
        ],
    )(factors, exposures, strikes.reshape(1, trades), notionals.reshape(1, trades))

def body(
    factors, exposures, strikes, notionals, w_first, b_first, w_second, b_second, w_out, b_out
):
    paths, width = factors.shape
    groups = lax.axis_size("trade")
    own_rows = paths // groups
    first_row = lax.axis_index("trade") * own_rows
    with jax.named_scope("price_trades"):
        packed = price(factors, exposures, strikes, notionals, own_rows)
    me = lax.axis_index("trade")
    z_len = groups // 2
    mine = lax.dynamic_index_in_dim(packed, me, 0, keepdims=False)
    for dy in range(2):
        for dz in range(z_len):
            if dy == 0 and dz == 0:
                continue

            def dest(t, dy=dy, dz=dz):
                return ((t // z_len + dy) % 2) * z_len + (t % z_len + dz) % z_len

            block = lax.dynamic_index_in_dim(packed, dest(me), 0, keepdims=False)
            mine = mine + lax.ppermute(block, "trade", [(t, dest(t)) for t in range(groups)])
    my_diff = mine[:own_rows]
    my_value = mine[own_rows : own_rows + own_rows // width].reshape(-1)
    my_inputs = lax.dynamic_slice_in_dim(factors, first_row, own_rows, 0).astype(jnp.float32)
    scale = 1.0 / jnp.sqrt(jnp.float32(paths * lax.axis_size("path")))
    params = (w_first, b_first, w_second, b_second, w_out, b_out)
    grads = jax.grad(twin_loss)(params, my_inputs, my_value, my_diff, scale)
    hidden = w_second.shape[0]
    small = jnp.stack([grads[1], grads[3], grads[4], jnp.pad(grads[5], (0, hidden - 1))])
    head = jnp.concatenate([grads[0], small], axis=0)
    head, g2 = lax.psum((head, grads[2]), ("path", "trade"))
    n0 = w_first.shape[0]
    g0 = head[:n0]
    tail = head[n0:]
    return (g0, tail[0], g2, tail[1], tail[2], tail[3, :1])

def solution(mesh):
    in_specs = (
        P("path", None),
        P("trade", None),
        P("trade"),
        P("trade"),
        P(),
        P(),
        P(),
        P(),
        P(),
        P(),
    )
    out_specs = (P(), P(), P(), P(), P(), P())
    return jax.shard_map(body, mesh=mesh, in_specs=in_specs, out_specs=out_specs, check_vma=False)
```

```python
import jax
import jax.numpy as jnp
from jax import lax
from jax.sharding import PartitionSpec as P
from jax.experimental import pallas as pl
from jax.experimental.pallas import tpu as pltpu


def twin_loss(params, inputs, value, differential, scale):
    w_first, b_first, w_second, b_second, w_out, b_out = params
    highest = lax.Precision.HIGH
    act_one = jnp.dot(inputs, w_first, precision=highest) + b_first
    hid_one = jax.nn.softplus(act_one)
    act_two = jnp.dot(hid_one, w_second, precision=highest) + b_second
    hid_two = jax.nn.softplus(act_two)
    predicted = jnp.dot(hid_two, w_out, precision=highest) + b_out[0]
    back_two = w_out * jax.nn.sigmoid(act_two)
    back_one = jnp.dot(back_two, w_second.T, precision=highest) * jax.nn.sigmoid(act_one)
    slope = jnp.dot(back_one, w_first.T, precision=highest)
    miss_value = predicted - value
    miss_slope = slope - differential
    return (jnp.sum(miss_value * miss_value) + jnp.sum(miss_slope * miss_slope)) * scale


ROW_CHUNK = 32
LANE_CHUNK = 128


def price_kernel(f_ref, e_ref, s_ref, n_ref, d_ref, m_scr, w_scr, v_scr):
    m_scr[...] = lax.dot_general(
        f_ref[...], e_ref[...], (((1,), (1,)), ((), ())), preferred_element_type=jnp.float32
    )
    tile, trades = m_scr.shape

    def rows(i, carry):
        r = pl.multiple_of(i * ROW_CHUNK, ROW_CHUNK)
        acc = jnp.zeros((ROW_CHUNK, 128), jnp.float32)
        for c in range(trades // LANE_CHUNK):
            cs = slice(c * LANE_CHUNK, (c + 1) * LANE_CHUNK)
            m = m_scr[pl.ds(r, ROW_CHUNK), cs] - s_ref[:, cs]
            notional = n_ref[:, cs]
            e = jnp.exp(-jnp.abs(m))
            soft = jnp.maximum(m, 0.0) + jnp.log1p(e)
            sig = jnp.exp(m - soft)
            w_scr[pl.ds(r, ROW_CHUNK), cs] = (sig * notional).astype(jnp.bfloat16)
            t = soft * notional
            for g in range(LANE_CHUNK // 128):
                acc = acc + t[:, g * 128 : (g + 1) * 128]
        v_scr[pl.ds(r, ROW_CHUNK), :] = acc
        return carry

    lax.fori_loop(0, tile // ROW_CHUNK, rows, 0)
    width = e_ref.shape[1]
    d_ref[0, :tile, :] = jnp.dot(w_scr[...], e_ref[...], preferred_element_type=jnp.float32)
    value = jnp.sum(jnp.transpose(v_scr[...]), axis=0, keepdims=True)
    d_ref[0, tile:, :] = jnp.zeros((d_ref.shape[1] - tile, width), jnp.float32)
    for k in range(tile // width):
        d_ref[0, tile + k : tile + k + 1, :] = value[:, k * width : (k + 1) * width]


def price(factors, exposures, strikes, notionals, tile):
    paths, width = factors.shape
    trades = exposures.shape[0]
    extra = -(-(tile // width) // 8) * 8
    return pl.pallas_call(
        price_kernel,
        grid=(paths // tile,),
        in_specs=[
            pl.BlockSpec((tile, width), lambda i: (i, 0)),
            pl.BlockSpec((trades, width), lambda i: (0, 0)),
            pl.BlockSpec((1, trades), lambda i: (0, 0)),
            pl.BlockSpec((1, trades), lambda i: (0, 0)),
        ],
        out_specs=pl.BlockSpec((1, tile + extra, width), lambda i: (i, 0, 0)),
        out_shape=jax.ShapeDtypeStruct((paths // tile, tile + extra, width), jnp.float32),
        scratch_shapes=[
            pltpu.VMEM((tile, trades), jnp.float32),
            pltpu.VMEM((tile, trades), jnp.bfloat16),
            pltpu.VMEM((tile, 128), jnp.float32),
        ],
    )(factors, exposures, strikes.reshape(1, trades), notionals.reshape(1, trades))

def body(
    factors, exposures, strikes, notionals, w_first, b_first, w_second, b_second, w_out, b_out
):
    paths, width = factors.shape
    groups = lax.axis_size("trade")
    own_rows = paths // groups
    first_row = lax.axis_index("trade") * own_rows
    with jax.named_scope("price_trades"):
        packed = price(factors, exposures, strikes, notionals, own_rows)
    me = lax.axis_index("trade")
    z_len = groups // 2
    mine = lax.dynamic_index_in_dim(packed, me, 0, keepdims=False)
    for dy in range(2):
        for dz in range(z_len):
            if dy == 0 and dz == 0:
                continue

            def dest(t, dy=dy, dz=dz):
                return ((t // z_len + dy) % 2) * z_len + (t % z_len + dz) % z_len

            block = lax.dynamic_index_in_dim(packed, dest(me), 0, keepdims=False)
            mine = mine + lax.ppermute(block, "trade", [(t, dest(t)) for t in range(groups)])
    my_diff = mine[:own_rows]
    my_value = mine[own_rows : own_rows + own_rows // width].reshape(-1)
    my_inputs = lax.dynamic_slice_in_dim(factors, first_row, own_rows, 0).astype(jnp.float32)
    scale = 1.0 / jnp.sqrt(jnp.float32(paths * lax.axis_size("path")))
    params = (w_first, b_first, w_second, b_second, w_out, b_out)
    grads = jax.grad(twin_loss)(params, my_inputs, my_value, my_diff, scale)
    hidden = w_second.shape[0]
    small = jnp.stack([grads[1], grads[3], grads[4], jnp.pad(grads[5], (0, hidden - 1))])
    head = jnp.concatenate([grads[0], small], axis=0)
    head, g2 = lax.psum((head, grads[2]), ("path", "trade"))
    n0 = w_first.shape[0]
    g0 = head[:n0]
    tail = head[n0:]
    return (g0, tail[0], g2, tail[1], tail[2], tail[3, :1])

def solution(mesh):
    in_specs = (
        P("path", None),
        P("trade", None),
        P("trade"),
        P("trade"),
        P(),
        P(),
        P(),
        P(),
        P(),
        P(),
    )
    out_specs = (P(), P(), P(), P(), P(), P())
    return jax.shard_map(body, mesh=mesh, in_specs=in_specs, out_specs=out_specs, check_vma=False)
```

```python
import jax
import jax.numpy as jnp
from jax import lax
from jax.sharding import PartitionSpec as P
from jax.experimental import pallas as pl
from jax.experimental.pallas import tpu as pltpu


def twin_loss(params, inputs, value, differential, scale):
    w_first, b_first, w_second, b_second, w_out, b_out = params
    highest = lax.Precision.HIGH
    act_one = jnp.dot(inputs, w_first, precision=highest) + b_first
    hid_one = jax.nn.softplus(act_one)
    act_two = jnp.dot(hid_one, w_second, precision=highest) + b_second
    hid_two = jax.nn.softplus(act_two)
    predicted = jnp.dot(hid_two, w_out, precision=highest) + b_out[0]
    back_two = w_out * jax.nn.sigmoid(act_two)
    back_one = jnp.dot(back_two, w_second.T, precision=highest) * jax.nn.sigmoid(act_one)
    slope = jnp.dot(back_one, w_first.T, precision=highest)
    miss_value = predicted - value
    miss_slope = slope - differential
    return (jnp.sum(miss_value * miss_value) + jnp.sum(miss_slope * miss_slope)) * scale


ROW_CHUNK = 64
LANE_CHUNK = 128


def price_kernel(f_ref, e_ref, s_ref, n_ref, d_ref, m_scr, w_scr, v_scr):
    m_scr[...] = lax.dot_general(
        f_ref[...], e_ref[...], (((1,), (1,)), ((), ())), preferred_element_type=jnp.float32
    )
    tile, trades = m_scr.shape

    def rows(i, carry):
        r = pl.multiple_of(i * ROW_CHUNK, ROW_CHUNK)
        acc = jnp.zeros((ROW_CHUNK, 128), jnp.float32)
        for c in range(trades // LANE_CHUNK):
            cs = slice(c * LANE_CHUNK, (c + 1) * LANE_CHUNK)
            m = m_scr[pl.ds(r, ROW_CHUNK), cs] - s_ref[:, cs]
            notional = n_ref[:, cs]
            e = jnp.exp(-jnp.abs(m))
            soft = jnp.maximum(m, 0.0) + jnp.log1p(e)
            sig = jnp.exp(m - soft)
            w_scr[pl.ds(r, ROW_CHUNK), cs] = (sig * notional).astype(jnp.bfloat16)
            t = soft * notional
            for g in range(LANE_CHUNK // 128):
                acc = acc + t[:, g * 128 : (g + 1) * 128]
        v_scr[pl.ds(r, ROW_CHUNK), :] = acc
        return carry

    lax.fori_loop(0, tile // ROW_CHUNK, rows, 0)
    width = e_ref.shape[1]
    d_ref[0, :tile, :] = jnp.dot(w_scr[...], e_ref[...], preferred_element_type=jnp.float32)
    value = jnp.sum(jnp.transpose(v_scr[...]), axis=0, keepdims=True)
    d_ref[0, tile:, :] = jnp.zeros((d_ref.shape[1] - tile, width), jnp.float32)
    for k in range(tile // width):
        d_ref[0, tile + k : tile + k + 1, :] = value[:, k * width : (k + 1) * width]


def price(factors, exposures, strikes, notionals, tile):
    paths, width = factors.shape
    trades = exposures.shape[0]
    extra = -(-(tile // width) // 8) * 8
    return pl.pallas_call(
        price_kernel,
        grid=(paths // tile,),
        in_specs=[
            pl.BlockSpec((tile, width), lambda i: (i, 0)),
            pl.BlockSpec((trades, width), lambda i: (0, 0)),
            pl.BlockSpec((1, trades), lambda i: (0, 0)),
            pl.BlockSpec((1, trades), lambda i: (0, 0)),
        ],
        out_specs=pl.BlockSpec((1, tile + extra, width), lambda i: (i, 0, 0)),
        out_shape=jax.ShapeDtypeStruct((paths // tile, tile + extra, width), jnp.float32),
        scratch_shapes=[
            pltpu.VMEM((tile, trades), jnp.float32),
            pltpu.VMEM((tile, trades), jnp.bfloat16),
            pltpu.VMEM((tile, 128), jnp.float32),
        ],
    )(factors, exposures, strikes.reshape(1, trades), notionals.reshape(1, trades))

def body(
    factors, exposures, strikes, notionals, w_first, b_first, w_second, b_second, w_out, b_out
):
    paths, width = factors.shape
    groups = lax.axis_size("trade")
    own_rows = paths // groups
    first_row = lax.axis_index("trade") * own_rows
    with jax.named_scope("price_trades"):
        packed = price(factors, exposures, strikes, notionals, own_rows)
    me = lax.axis_index("trade")
    z_len = groups // 2
    mine = lax.dynamic_index_in_dim(packed, me, 0, keepdims=False)
    for dy in range(2):
        for dz in range(z_len):
            if dy == 0 and dz == 0:
                continue

            def dest(t, dy=dy, dz=dz):
                return ((t // z_len + dy) % 2) * z_len + (t % z_len + dz) % z_len

            block = lax.dynamic_index_in_dim(packed, dest(me), 0, keepdims=False)
            mine = mine + lax.ppermute(block, "trade", [(t, dest(t)) for t in range(groups)])
    my_diff = mine[:own_rows]
    my_value = mine[own_rows : own_rows + own_rows // width].reshape(-1)
    my_inputs = lax.dynamic_slice_in_dim(factors, first_row, own_rows, 0).astype(jnp.float32)
    scale = 1.0 / jnp.sqrt(jnp.float32(paths * lax.axis_size("path")))
    params = (w_first, b_first, w_second, b_second, w_out, b_out)
    grads = jax.grad(twin_loss)(params, my_inputs, my_value, my_diff, scale)
    hidden = w_second.shape[0]
    small = jnp.stack([grads[1], grads[3], grads[4], jnp.pad(grads[5], (0, hidden - 1))])
    head = jnp.concatenate([grads[0], small], axis=0)
    head, g2 = lax.psum((head, grads[2]), ("path", "trade"))
    n0 = w_first.shape[0]
    g0 = head[:n0]
    tail = head[n0:]
    return (g0, tail[0], g2, tail[1], tail[2], tail[3, :1])

def solution(mesh):
    in_specs = (
        P("path", None),
        P("trade", None),
        P("trade"),
        P("trade"),
        P(),
        P(),
        P(),
        P(),
        P(),
        P(),
    )
    out_specs = (P(), P(), P(), P(), P(), P())
    return jax.shard_map(body, mesh=mesh, in_specs=in_specs, out_specs=out_specs, check_vma=False)
```

```python
import jax
import jax.numpy as jnp
from jax import lax
from jax.sharding import PartitionSpec as P
from jax.experimental import pallas as pl
from jax.experimental.pallas import tpu as pltpu


def twin_loss(params, inputs, value, differential, scale):
    w_first, b_first, w_second, b_second, w_out, b_out = params
    highest = lax.Precision.HIGH
    act_one = jnp.dot(inputs, w_first, precision=highest) + b_first
    hid_one = jax.nn.softplus(act_one)
    act_two = jnp.dot(hid_one, w_second, precision=highest) + b_second
    hid_two = jax.nn.softplus(act_two)
    predicted = jnp.dot(hid_two, w_out, precision=highest) + b_out[0]
    back_two = w_out * jax.nn.sigmoid(act_two)
    back_one = jnp.dot(back_two, w_second.T, precision=highest) * jax.nn.sigmoid(act_one)
    slope = jnp.dot(back_one, w_first.T, precision=highest)
    miss_value = predicted - value
    miss_slope = slope - differential
    return (jnp.sum(miss_value * miss_value) + jnp.sum(miss_slope * miss_slope)) * scale


ROW_CHUNK = 16
LANE_CHUNK = 128


def price_kernel(f_ref, e_ref, s_ref, n_ref, d_ref, m_scr, w_scr, v_scr):
    m_scr[...] = lax.dot_general(
        f_ref[...], e_ref[...], (((1,), (1,)), ((), ())), preferred_element_type=jnp.float32
    )
    tile, trades = m_scr.shape

    def rows(i, carry):
        r = pl.multiple_of(i * ROW_CHUNK, ROW_CHUNK)
        acc = jnp.zeros((ROW_CHUNK, 128), jnp.float32)
        for c in range(trades // LANE_CHUNK):
            cs = slice(c * LANE_CHUNK, (c + 1) * LANE_CHUNK)
            m = m_scr[pl.ds(r, ROW_CHUNK), cs] - s_ref[:, cs]
            notional = n_ref[:, cs]
            e = jnp.exp(-jnp.abs(m))
            soft = jnp.maximum(m, 0.0) + jnp.log1p(e)
            sig = jnp.exp(m - soft)
            w_scr[pl.ds(r, ROW_CHUNK), cs] = (sig * notional).astype(jnp.bfloat16)
            t = soft * notional
            for g in range(LANE_CHUNK // 128):
                acc = acc + t[:, g * 128 : (g + 1) * 128]
        v_scr[pl.ds(r, ROW_CHUNK), :] = acc
        return carry

    lax.fori_loop(0, tile // ROW_CHUNK, rows, 0)
    width = e_ref.shape[1]
    d_ref[0, :tile, :] = jnp.dot(w_scr[...], e_ref[...], preferred_element_type=jnp.float32)
    value = jnp.sum(jnp.transpose(v_scr[...]), axis=0, keepdims=True)
    d_ref[0, tile:, :] = jnp.zeros((d_ref.shape[1] - tile, width), jnp.float32)
    for k in range(tile // width):
        d_ref[0, tile + k : tile + k + 1, :] = value[:, k * width : (k + 1) * width]


def price(factors, exposures, strikes, notionals, tile):
    paths, width = factors.shape
    trades = exposures.shape[0]
    extra = -(-(tile // width) // 8) * 8
    return pl.pallas_call(
        price_kernel,
        grid=(paths // tile,),
        in_specs=[
            pl.BlockSpec((tile, width), lambda i: (i, 0)),
            pl.BlockSpec((trades, width), lambda i: (0, 0)),
            pl.BlockSpec((1, trades), lambda i: (0, 0)),
            pl.BlockSpec((1, trades), lambda i: (0, 0)),
        ],
        out_specs=pl.BlockSpec((1, tile + extra, width), lambda i: (i, 0, 0)),
        out_shape=jax.ShapeDtypeStruct((paths // tile, tile + extra, width), jnp.float32),
        scratch_shapes=[
            pltpu.VMEM((tile, trades), jnp.float32),
            pltpu.VMEM((tile, trades), jnp.bfloat16),
            pltpu.VMEM((tile, 128), jnp.float32),
        ],
    )(factors, exposures, strikes.reshape(1, trades), notionals.reshape(1, trades))

def body(
    factors, exposures, strikes, notionals, w_first, b_first, w_second, b_second, w_out, b_out
):
    paths, width = factors.shape
    groups = lax.axis_size("trade")
    own_rows = paths // groups
    first_row = lax.axis_index("trade") * own_rows
    with jax.named_scope("price_trades"):
        packed = price(factors, exposures, strikes, notionals, own_rows)
    me = lax.axis_index("trade")
    z_len = groups // 2
    mine = lax.dynamic_index_in_dim(packed, me, 0, keepdims=False)
    for dy in range(2):
        for dz in range(z_len):
            if dy == 0 and dz == 0:
                continue

            def dest(t, dy=dy, dz=dz):
                return ((t // z_len + dy) % 2) * z_len + (t % z_len + dz) % z_len

            block = lax.dynamic_index_in_dim(packed, dest(me), 0, keepdims=False)
            mine = mine + lax.ppermute(block, "trade", [(t, dest(t)) for t in range(groups)])
    my_diff = mine[:own_rows]
    my_value = mine[own_rows : own_rows + own_rows // width].reshape(-1)
    my_inputs = lax.dynamic_slice_in_dim(factors, first_row, own_rows, 0).astype(jnp.float32)
    scale = 1.0 / jnp.sqrt(jnp.float32(paths * lax.axis_size("path")))
    params = (w_first, b_first, w_second, b_second, w_out, b_out)
    grads = jax.grad(twin_loss)(params, my_inputs, my_value, my_diff, scale)
    hidden = w_second.shape[0]
    small = jnp.stack([grads[1], grads[3], grads[4], jnp.pad(grads[5], (0, hidden - 1))])
    head = jnp.concatenate([grads[0], small], axis=0)
    head, g2 = lax.psum((head, grads[2]), ("path", "trade"))
    n0 = w_first.shape[0]
    g0 = head[:n0]
    tail = head[n0:]
    return (g0, tail[0], g2, tail[1], tail[2], tail[3, :1])

def solution(mesh):
    in_specs = (
        P("path", None),
        P("trade", None),
        P("trade"),
        P("trade"),
        P(),
        P(),
        P(),
        P(),
        P(),
        P(),
    )
    out_specs = (P(), P(), P(), P(), P(), P())
    return jax.shard_map(body, mesh=mesh, in_specs=in_specs, out_specs=out_specs, check_vma=False)
```
